256 devices in a mesh: dp: 16 (over y_lo, z), fsdp: 16 (over x, y_hi, core).
Axes of the slice: x: 4, y: 4 (y_hi: 2, y_lo: 2; y = y_hi * 2 + y_lo), z: 8, core: 2. Of those that a mesh axis runs over, the one named last changes fastest.
Arguments:
- latents: bfloat16 [1024, 8, 8, 640], P(('dp', 'fsdp'))
- bucket: int32 [1024], P(('dp', 'fsdp')), may hold values from 0 to 39
- cotangent: bfloat16 [1024, 4, 4, 640], P(('dp', 'fsdp')), may hold values from -6 to 6
- tile_count: int32 [256], P(('dp', 'fsdp')), may hold values from 1 to 4, as said below
- cond_table: float32 [40, 640], replicated, may hold values from -3 to 3
- norm_gain: float32 [640], replicated, may hold values from 0.1 to 1.9
- norm_shift: float32 [640], replicated, may hold values from -3 to 3
- conv_bias: float32 [640], replicated, may hold values from -3 to 3
- down_bias: float32 [640], replicated, may hold values from -3 to 3
- conv_weight: bfloat16 [5760, 640], P('fsdp'), may hold values from -0.078125 to 0.078125
- down_weight: bfloat16 [5760, 640], P('fsdp'), may hold values from -0.078125 to 0.078125
Outputs:
- block_output: bfloat16 [1024, 4, 4, 640], P(('dp', 'fsdp'))
- grad_input: bfloat16 [1024, 8, 8, 640], P(('dp', 'fsdp'))
- grad_conv: float32 [5760, 640], P('fsdp')
- grad_affine: float32 [3, 640], replicated
The draws below stay inside these ranges and needn't reach their ends.
Inputs may be any that keep to these rules, and one draw needn't show every extreme that they name: Slots 0 to tile_count - 1 of a device are live; some device holds exactly 4 live tiles.
All inputs are finite; a program needn't handle non-finite values.
Results may differ from the reference program's by a relative error of at most 0.005.
Values may be sent and summed in bfloat16 or wider, within the bound.
No kernel may reach another device: no remote copies, remote signals or barrier semaphores. Data moves between devices by JAX's collectives and lax.ppermute only.
A program may use at most 128 MiB of HBM per device.

```python
import math
import jax
import jax.numpy as jnp
import numpy as np
from jax import lax

C = 640
GROUPS = 32
S = 8
CAP = 4
NB = 40
S2 = 4
KC = 5760
WORKERS = 256
TILES = 1024
N_DP = 16
N_FSDP = 16


def draw_latents(key, part):
    key_base, key_rows, key_chan, key_shift = jax.random.split(key, 4)
    spread = math.log(10.0)
    values = jax.random.normal(key_base, (TILES, S, S, C), jnp.float32)
    offset = 0.5 * jax.random.normal(key_shift, (TILES, 1, 1, C), jnp.float32)
    row_scale = 0.15 * jnp.exp(jax.random.uniform(key_rows, (TILES, S, S, 1), jnp.float32, 0.0, spread))
    chan_scale = 0.15 * jnp.exp(jax.random.uniform(key_chan, (C,), jnp.float32, 0.0, spread))
    return (values * row_scale * chan_scale + offset).astype(jnp.bfloat16)


def draw_tile_count(key, part):
    key_base, key_heavy, key_pick = jax.random.split(key, 3)
    base_count = jax.random.randint(key_base, (WORKERS,), 1, CAP // 2 + 1)
    heavy = jax.random.randint(key_heavy, (WORKERS,), 0, 16) == 0
    picked = jax.random.randint(key_pick, (), 0, WORKERS)
    full_load = heavy | (jnp.arange(WORKERS) == picked)
    return jnp.where(full_load, CAP, base_count).astype(jnp.int32)


def set_ends(drawn, key, smallest, high):
    longest = drawn.shape.index(max(drawn.shape))
    spots = []
    for shift in (0, 1):
        where = [jax.random.randint(jax.random.fold_in(key, axis), (), 0, length) for axis, length in enumerate(drawn.shape)]
        where[longest] = (where[longest] + shift) % drawn.shape[longest]
        spots.append(tuple(where))
    return drawn.at[spots[0]].set(smallest).at[spots[1]].set(high)


def steps_of(own_key, shape, cuts, smallest, largest):
    gain, own = 1.0, jax.random.fold_in(own_key, 6)
    for axis_at, shards_of in cuts:
        draws = jnp.exp(jax.random.uniform(jax.random.fold_in(own, axis_at), (shards_of,), jnp.float32, smallest / len(cuts), largest / len(cuts)))
        gain = gain * jnp.repeat(draws, shape[axis_at] // shards_of).reshape([-1 if axis == axis_at else 1 for axis in range(len(shape))])
    return gain


def rank_bounds(amount, lean):
    weights = [(1 << 20) // math.isqrt(rank ** lean) + 1 for rank in range(1, amount + 1)]
    scale = 1 + sum(weights) // (1 << 30)
    return np.cumsum(np.array([max(1, weight // scale) for weight in weights]))


def ranked(rng, dims, count, slope):
    grid = rank_bounds(count, slope)
    pick = jax.random.randint(jax.random.fold_in(rng, 1), dims, 0, int(grid[count - 1]))
    grade = jnp.searchsorted(jnp.asarray(grid, jnp.int32), pick, side="right")
    return jax.random.permutation(jax.random.fold_in(rng, 2), count)[grade].astype(jnp.int32)


def bell_draw(key, shape, scale, bound, cuts=(), kind=jnp.bfloat16):
    result = scale * jax.random.normal(key, shape, jnp.float32)
    if cuts:
        result = result * steps_of(key, shape, cuts, -0.22, 0.18)
    return jnp.clip(result, -bound, bound).astype(kind)


def setup_inputs(seed: int = 0) -> dict:
    seeds = jax.random.split(jax.random.key(seed), 12)
    return {
        "latents": draw_latents(jax.random.fold_in(seeds[11], 71), 0),
        "bucket": set_ends(ranked(seeds[1], (TILES,), NB, 2), jax.random.fold_in(seeds[1], 3), 0, NB - 1).astype(jnp.int32),
        "cotangent": bell_draw(seeds[2], (TILES, S2, S2, C), 1.0, 6.0, ((0, 256),)),
        "tile_count": draw_tile_count(jax.random.fold_in(seeds[11], 71), 0),
        "cond_table": bell_draw(seeds[4], (NB, C), 0.5, 3.0, (), jnp.float32),
        "norm_gain": jnp.clip(1.0 + 0.18 * jax.random.normal(seeds[5], (C,), jnp.float32), 0.1, 1.9),
        "norm_shift": bell_draw(seeds[6], (C,), 0.5, 3.0, (), jnp.float32),
        "conv_bias": bell_draw(seeds[7], (C,), 0.5, 3.0, (), jnp.float32),
        "down_bias": bell_draw(seeds[8], (C,), 0.5, 3.0, (), jnp.float32),
        "conv_weight": bell_draw(seeds[9], (KC, C), KC ** -0.5, 0.078125, ((0, 16),)),
        "down_weight": bell_draw(seeds[10], (KC, C), KC ** -0.5, 0.078125, ((0, 16),)),
    }


def tap_patches(values):
    tile_side = values.shape[1]
    channels = values.shape[3]
    padded = jnp.pad(values, ((0, 0), (1, 1), (1, 1), (0, 0)))
    pieces = [padded[:, row_off:row_off + tile_side, col_off:col_off + tile_side, :] for row_off in range(3) for col_off in range(3)]
    return jnp.concatenate(pieces, axis=-1).reshape(-1, 9 * channels)

def down_patches(values):
    tile_side = values.shape[1]
    channels = values.shape[3]
    padded = jnp.pad(values, ((0, 0), (1, 1), (1, 1), (0, 0)))
    pieces = [padded[:, row_off:row_off + tile_side - 1:2, col_off:col_off + tile_side - 1:2, :] for row_off in range(3) for col_off in range(3)]
    return jnp.concatenate(pieces, axis=-1).reshape(-1, 9 * channels)

def fold_taps(grads, tile_side, stride):
    tile_total = grads.shape[0]
    channels = grads.shape[3] // 9
    padded = jnp.zeros((tile_total, tile_side + 2, tile_side + 2, channels), jnp.float32)
    for tap_index in range(9):
        row_off = tap_index // 3
        col_off = tap_index % 3
        stop_row = row_off + tile_side - (stride - 1)
        stop_col = col_off + tile_side - (stride - 1)
        padded = padded.at[:, row_off:stop_row:stride, col_off:stop_col:stride, :].add(grads[..., tap_index * channels:(tap_index + 1) * channels])
    return padded[:, 1:tile_side + 1, 1:tile_side + 1, :]

def group_mean(channel_sums, member, per_group):
    grouped = jnp.dot(channel_sums, member, precision=lax.Precision.HIGHEST) / per_group
    return jnp.dot(grouped, jnp.transpose(member), precision=lax.Precision.HIGHEST)

def tile_pass(latent_block, bucket_block, cotangent_block, params):
    cond_table, norm_gain, norm_shift, conv_bias, down_bias, conv_full, down_full = params
    tile_total = latent_block.shape[0]
    tile_side = latent_block.shape[1]
    channels = latent_block.shape[3]
    half_side = tile_side // 2
    member = (jnp.arange(channels, dtype=jnp.int32)[:, None] // (channels // GROUPS) == jnp.arange(GROUPS, dtype=jnp.int32)[None, :]).astype(jnp.float32)
    per_group = tile_side * tile_side * (channels // GROUPS)
    values = latent_block.astype(jnp.float32)
    center = group_mean(lax.optimization_barrier(jnp.sum(values, axis=(1, 2))), member, per_group)
    deviation = values - center[:, None, None, :]
    spread = group_mean(lax.optimization_barrier(jnp.sum(deviation * deviation, axis=(1, 2))), member, per_group)
    inv_std = lax.rsqrt(spread + 1e-05)[:, None, None, :]
    normed = deviation * inv_std
    pre_act = normed * norm_gain + norm_shift
    sigmoid_v = jax.nn.sigmoid(pre_act)
    activated = (pre_act * sigmoid_v).astype(jnp.bfloat16)
    onehot = (bucket_block[:, None] == jnp.arange(cond_table.shape[0], dtype=jnp.int32)[None, :]).astype(jnp.float32)
    conditioning = jnp.dot(onehot, cond_table, precision=lax.Precision.HIGHEST)
    conv_out = jnp.dot(tap_patches(activated), conv_full, preferred_element_type=jnp.float32).reshape(tile_total, tile_side, tile_side, channels)
    conv_out = conv_out + conv_bias + conditioning[:, None, None, :]
    residual = (values + conv_out).astype(jnp.bfloat16)
    down_out = jnp.dot(down_patches(residual), down_full, preferred_element_type=jnp.float32).reshape(tile_total, half_side, half_side, channels)
    block_output = (down_out + down_bias).astype(jnp.bfloat16)
    back_down = lax.dot_general(cotangent_block.reshape(-1, channels), down_full, (((1,), (1,)), ((), ())), preferred_element_type=jnp.float32)
    grad_resid = fold_taps(back_down.reshape(tile_total, half_side, half_side, 9 * channels), tile_side, 2)
    grad_hidden = grad_resid.astype(jnp.bfloat16)
    back_conv = lax.dot_general(grad_hidden.reshape(-1, channels), conv_full, (((1,), (1,)), ((), ())), preferred_element_type=jnp.float32)
    grad_act = fold_taps(back_conv.reshape(tile_total, tile_side, tile_side, 9 * channels), tile_side, 1)
    grad_pre = grad_act * sigmoid_v * (1.0 + pre_act * (1.0 - sigmoid_v))
    scaled = grad_pre * norm_gain
    mean_one = group_mean(lax.optimization_barrier(jnp.sum(scaled, axis=(1, 2))), member, per_group)[:, None, None, :]
    mean_two = group_mean(lax.optimization_barrier(jnp.sum(scaled * normed, axis=(1, 2))), member, per_group)[:, None, None, :]
    grad_input = (grad_resid + inv_std * (scaled - mean_one - normed * mean_two)).astype(jnp.bfloat16)
    affine = jnp.stack([lax.optimization_barrier(jnp.sum(grad_pre * normed, axis=(0, 1, 2))), lax.optimization_barrier(jnp.sum(grad_pre, axis=(0, 1, 2))), lax.optimization_barrier(jnp.sum(grad_resid, axis=(0, 1, 2)))])
    return (block_output, grad_input, activated, grad_hidden, affine)

def reference(latents, bucket, cotangent, tile_count, cond_table, norm_gain, norm_shift, conv_bias, down_bias, conv_weight, down_weight):
    workers = N_DP * N_FSDP
    params = (cond_table, norm_gain, norm_shift, conv_bias, down_bias, conv_weight, down_weight)
    live_slot = jnp.arange(CAP, dtype=jnp.int32)[None, :] < tile_count[:, None]
    latent_split = latents.reshape(workers, CAP, S, S, C)
    bucket_split = bucket.reshape(workers, CAP)
    cot_split = cotangent.reshape(workers, CAP, S2, S2, C)

    def per_worker(running, worker_item):
        latent_block, bucket_block, cot_block, live_block = worker_item
        masked_cot = jnp.where(live_block[:, None, None, None], cot_block, jnp.zeros_like(cot_block))
        block_output, grad_input, activated, grad_hidden, affine = tile_pass(latent_block, bucket_block, masked_cot, params)
        weight_term = lax.dot_general(tap_patches(activated), grad_hidden.reshape(-1, C), (((0,), (0,)), ((), ())), preferred_element_type=jnp.float32)
        block_output = jnp.where(live_block[:, None, None, None], block_output, jnp.zeros_like(block_output))
        return ((running[0] + weight_term, running[1] + affine), (block_output, grad_input))
    start_state = (jnp.zeros((KC, C), jnp.float32), jnp.zeros((3, C), jnp.float32))
    totals, stacked = lax.scan(per_worker, start_state, (latent_split, bucket_split, cot_split, live_slot))
    loss_scale = 4.0 / math.sqrt(S * S * TILES)
    return (stacked[0].reshape(TILES, S2, S2, C), stacked[1].reshape(TILES, S, S, C), totals[0] * loss_scale, totals[1] * loss_scale)
```

```python
import math

import jax
import jax.numpy as jnp
from jax import lax
from jax.sharding import PartitionSpec as P

GROUPS = 32
CONV_DIMS = ("NHWC", "HWIO", "NHWC")
BACK_DIMS = ("NHWC", "HWOI", "NHWC")


def group_mean(channel_sums, per_group):
    tiles, channels = channel_sums.shape
    width = channels // GROUPS
    grouped = channel_sums.reshape(tiles, GROUPS, width).sum(axis=-1) / per_group
    return jnp.repeat(grouped, width, axis=1)


def shifted(padded, tap, tile_side):
    row_off = tap // 3
    col_off = tap % 3
    return lax.dynamic_slice(
        padded,
        (0, row_off, col_off, 0),
        (padded.shape[0], tile_side, tile_side, padded.shape[3]),
    )


def body(
    latents,
    bucket,
    cotangent,
    tile_count,
    cond_table,
    norm_gain,
    norm_shift,
    conv_bias,
    down_bias,
    conv_weight,
    down_weight,
):
    slot_total, tile_side, _, channels = latents.shape
    row_block = conv_weight.shape[0]
    conv_full = lax.all_gather(conv_weight, "fsdp", axis=0, tiled=True)
    down_full = lax.all_gather(down_weight, "fsdp", axis=0, tiled=True)
    conv_kernel = conv_full.reshape(3, 3, channels, channels)
    down_kernel = down_full.reshape(3, 3, channels, channels)

    live = jnp.arange(slot_total, dtype=jnp.int32) < tile_count[0]
    live4 = live[:, None, None, None]
    masked_cot = jnp.where(live4, cotangent, jnp.zeros_like(cotangent))

    per_group = tile_side * tile_side * (channels // GROUPS)
    values = latents.astype(jnp.float32)
    center = group_mean(jnp.sum(values, axis=(1, 2)), per_group)
    deviation = values - center[:, None, None, :]
    spread = group_mean(jnp.sum(deviation * deviation, axis=(1, 2)), per_group)
    inv_std = lax.rsqrt(spread + 1e-05)[:, None, None, :]
    normed = deviation * inv_std
    pre_act = normed * norm_gain + norm_shift
    sigmoid_v = jax.nn.sigmoid(pre_act)
    activated = (pre_act * sigmoid_v).astype(jnp.bfloat16)
    act_all = lax.all_gather(activated, "fsdp", axis=0, tiled=True)

    conditioning = cond_table[bucket]
    conv_out = lax.conv_general_dilated(
        activated,
        conv_kernel,
        (1, 1),
        ((1, 1), (1, 1)),
        dimension_numbers=CONV_DIMS,
        preferred_element_type=jnp.float32,
    )
    conv_out = conv_out + conv_bias + conditioning[:, None, None, :]
    residual = (values + conv_out).astype(jnp.bfloat16)
    down_out = lax.conv_general_dilated(
        residual,
        down_kernel,
        (2, 2),
        ((1, 1), (1, 1)),
        dimension_numbers=CONV_DIMS,
        preferred_element_type=jnp.float32,
    )
    block_output = (down_out + down_bias).astype(jnp.bfloat16)
    block_output = jnp.where(live4, block_output, jnp.zeros_like(block_output))

    grad_resid = lax.conv_general_dilated(
        masked_cot,
        down_kernel[::-1, ::-1],
        (1, 1),
        ((1, 2), (1, 2)),
        lhs_dilation=(2, 2),
        dimension_numbers=BACK_DIMS,
        preferred_element_type=jnp.float32,
    )
    grad_hidden = grad_resid.astype(jnp.bfloat16)
    grad_act = lax.conv_general_dilated(
        grad_hidden,
        conv_kernel[::-1, ::-1],
        (1, 1),
        ((1, 1), (1, 1)),
        dimension_numbers=BACK_DIMS,
        preferred_element_type=jnp.float32,
    )
    grad_pre = grad_act * sigmoid_v * (1.0 + pre_act * (1.0 - sigmoid_v))
    scaled = grad_pre * norm_gain
    mean_one = group_mean(jnp.sum(scaled, axis=(1, 2)), per_group)[:, None, None, :]
    mean_two = group_mean(jnp.sum(scaled * normed, axis=(1, 2)), per_group)[:, None, None, :]
    grad_input = (grad_resid + inv_std * (scaled - mean_one - normed * mean_two)).astype(
        jnp.bfloat16
    )
    affine = jnp.stack(
        [
            jnp.sum(grad_pre * normed, axis=(0, 1, 2)),
            jnp.sum(grad_pre, axis=(0, 1, 2)),
            jnp.sum(grad_resid, axis=(0, 1, 2)),
        ]
    )
    affine_hi = affine.astype(jnp.bfloat16)
    affine_lo = (affine - affine_hi.astype(jnp.float32)).astype(jnp.bfloat16)
    hid_rows = grad_hidden.reshape(-1, channels)
    sent = jnp.concatenate([hid_rows, affine_hi, affine_lo], axis=0)
    sent_all = lax.all_gather(sent, "fsdp", axis=0, tiled=False)
    hid_all = sent_all[:, : hid_rows.shape[0]].reshape(-1, channels)
    affine_parts = sent_all[:, hid_rows.shape[0] :].astype(jnp.float32)
    affine_fsdp = jnp.sum(affine_parts[:, :3] + affine_parts[:, 3:], axis=0)

    first_row = lax.axis_index("fsdp") * row_block
    first_tap = first_row // channels
    first_chan = first_row % channels
    span = (row_block + channels - 1) // channels + 1
    act_pad = jnp.pad(act_all, ((0, 0), (1, 1), (1, 1), (0, 0)))
    taps = [
        shifted(act_pad, jnp.minimum(first_tap + extra, 8), tile_side) for extra in range(span)
    ]
    tap_cols = jnp.concatenate(taps, axis=-1)
    own_cols = lax.dynamic_slice_in_dim(tap_cols, first_chan, row_block, axis=3)
    weight_term = lax.dot_general(
        own_cols.reshape(-1, row_block),
        hid_all,
        (((0,), (0,)), ((), ())),
        preferred_element_type=jnp.float32,
    )
    loss_scale = 4.0 / math.sqrt(
        tile_side * tile_side * slot_total * lax.axis_size("dp") * lax.axis_size("fsdp")
    )
    summed = lax.psum(
        jnp.concatenate([weight_term, affine_fsdp], axis=0) * loss_scale, "dp"
    )
    grad_conv = summed[:row_block]
    grad_affine = summed[row_block:]
    return (block_output, grad_input, grad_conv, grad_affine)


def solution(mesh):
    placed = (
        P(("dp", "fsdp"), None, None, None),
        P(("dp", "fsdp")),
        P(("dp", "fsdp"), None, None, None),
        P(("dp", "fsdp")),
        P(),
        P(),
        P(),
        P(),
        P(),
        P("fsdp", None),
        P("fsdp", None),
    )
    return jax.shard_map(
        body,
        mesh=mesh,
        in_specs=placed,
        out_specs=(
            P(("dp", "fsdp"), None, None, None),
            P(("dp", "fsdp"), None, None, None),
            P("fsdp", None),
            P(),
        ),
        check_vma=False,
    )
```

```python
import math

import jax
import jax.numpy as jnp
from jax import lax
from jax.sharding import PartitionSpec as P

GROUPS = 32
CONV_DIMS = ("NHWC", "HWIO", "NHWC")
BACK_DIMS = ("NHWC", "HWOI", "NHWC")


def group_mean(channel_sums, per_group):
    tiles, channels = channel_sums.shape
    width = channels // GROUPS
    grouped = channel_sums.reshape(tiles, GROUPS, width).sum(axis=-1) / per_group
    return jnp.repeat(grouped, width, axis=1)


def shifted(padded, tap, tile_side):
    row_off = tap // 3
    col_off = tap % 3
    return lax.dynamic_slice(
        padded,
        (0, row_off, col_off, 0),
        (padded.shape[0], tile_side, tile_side, padded.shape[3]),
    )


def halving_doubling_sum(block, axis):
    size = lax.axis_size(axis)
    levels = size.bit_length() - 1
    if size != 1 << levels or levels == 0:
        return lax.psum(block, axis)
    order = [0, levels - 1] + list(range(1, levels - 1)) if levels > 1 else [0]
    rows = block.shape[0]
    padded_rows = -(-rows // size) * size
    cur = jnp.pad(block, ((0, padded_rows - rows), (0, 0)))
    index = lax.axis_index(axis)
    for level in order:
        half = cur.shape[0] // 2
        low = ((index >> level) & 1) == 0
        send = jnp.where(low, cur[half:], cur[:half])
        keep = jnp.where(low, cur[:half], cur[half:])
        pairs = [(i, i ^ (1 << level)) for i in range(size)]
        cur = keep + lax.ppermute(send, axis, pairs)
    for level in reversed(order):
        low = ((index >> level) & 1) == 0
        pairs = [(i, i ^ (1 << level)) for i in range(size)]
        other = lax.ppermute(cur, axis, pairs)
        cur = jnp.where(low, jnp.concatenate([cur, other]), jnp.concatenate([other, cur]))
    return cur[:rows]


def body(
    latents,
    bucket,
    cotangent,
    tile_count,
    cond_table,
    norm_gain,
    norm_shift,
    conv_bias,
    down_bias,
    conv_weight,
    down_weight,
):
    slot_total, tile_side, _, channels = latents.shape
    row_block = conv_weight.shape[0]
    conv_full = lax.all_gather(conv_weight, "fsdp", axis=0, tiled=True)
    down_full = lax.all_gather(down_weight, "fsdp", axis=0, tiled=True)
    conv_kernel = conv_full.reshape(3, 3, channels, channels)
    down_kernel = down_full.reshape(3, 3, channels, channels)

    live = jnp.arange(slot_total, dtype=jnp.int32) < tile_count[0]
    live4 = live[:, None, None, None]
    masked_cot = jnp.where(live4, cotangent, jnp.zeros_like(cotangent))

    per_group = tile_side * tile_side * (channels // GROUPS)
    values = latents.astype(jnp.float32)
    center = group_mean(jnp.sum(values, axis=(1, 2)), per_group)
    deviation = values - center[:, None, None, :]
    spread = group_mean(jnp.sum(deviation * deviation, axis=(1, 2)), per_group)
    inv_std = lax.rsqrt(spread + 1e-05)[:, None, None, :]
    normed = deviation * inv_std
    pre_act = normed * norm_gain + norm_shift
    sigmoid_v = jax.nn.sigmoid(pre_act)
    activated = (pre_act * sigmoid_v).astype(jnp.bfloat16)
    act_all = lax.all_gather(activated, "fsdp", axis=0, tiled=True)

    conditioning = cond_table[bucket]
    conv_out = lax.conv_general_dilated(
        activated,
        conv_kernel,
        (1, 1),
        ((1, 1), (1, 1)),
        dimension_numbers=CONV_DIMS,
        preferred_element_type=jnp.float32,
    )
    conv_out = conv_out + conv_bias + conditioning[:, None, None, :]
    residual = (values + conv_out).astype(jnp.bfloat16)
    down_out = lax.conv_general_dilated(
        residual,
        down_kernel,
        (2, 2),
        ((1, 1), (1, 1)),
        dimension_numbers=CONV_DIMS,
        preferred_element_type=jnp.float32,
    )
    block_output = (down_out + down_bias).astype(jnp.bfloat16)
    block_output = jnp.where(live4, block_output, jnp.zeros_like(block_output))

    cot_all = lax.all_gather(masked_cot, "fsdp", axis=0, tiled=True)
    resid_all = lax.conv_general_dilated(
        cot_all,
        down_kernel[::-1, ::-1],
        (1, 1),
        ((1, 2), (1, 2)),
        lhs_dilation=(2, 2),
        dimension_numbers=BACK_DIMS,
        preferred_element_type=jnp.float32,
    )
    hid_all = resid_all.astype(jnp.bfloat16).reshape(-1, channels)
    grad_resid = lax.dynamic_slice_in_dim(
        resid_all, lax.axis_index("fsdp") * slot_total, slot_total, axis=0
    )
    grad_hidden = grad_resid.astype(jnp.bfloat16)
    grad_act = lax.conv_general_dilated(
        grad_hidden,
        conv_kernel[::-1, ::-1],
        (1, 1),
        ((1, 1), (1, 1)),
        dimension_numbers=BACK_DIMS,
        preferred_element_type=jnp.float32,
    )
    grad_pre = grad_act * sigmoid_v * (1.0 + pre_act * (1.0 - sigmoid_v))
    scaled = grad_pre * norm_gain
    mean_one = group_mean(jnp.sum(scaled, axis=(1, 2)), per_group)[:, None, None, :]
    mean_two = group_mean(jnp.sum(scaled * normed, axis=(1, 2)), per_group)[:, None, None, :]
    grad_input = (grad_resid + inv_std * (scaled - mean_one - normed * mean_two)).astype(
        jnp.bfloat16
    )
    affine = jnp.stack(
        [
            jnp.sum(grad_pre * normed, axis=(0, 1, 2)),
            jnp.sum(grad_pre, axis=(0, 1, 2)),
            jnp.sum(grad_resid, axis=(0, 1, 2)),
        ]
    )
    affine_fsdp = lax.psum(affine, "fsdp")

    first_row = lax.axis_index("fsdp") * row_block
    first_tap = first_row // channels
    first_chan = first_row % channels
    span = (row_block + channels - 1) // channels + 1
    act_pad = jnp.pad(act_all, ((0, 0), (1, 1), (1, 1), (0, 0)))
    taps = [
        shifted(act_pad, jnp.minimum(first_tap + extra, 8), tile_side) for extra in range(span)
    ]
    tap_cols = jnp.concatenate(taps, axis=-1)
    own_cols = lax.dynamic_slice_in_dim(tap_cols, first_chan, row_block, axis=3)
    weight_term = lax.dot_general(
        own_cols.reshape(-1, row_block),
        hid_all,
        (((0,), (0,)), ((), ())),
        preferred_element_type=jnp.float32,
    )
    loss_scale = 4.0 / math.sqrt(
        tile_side * tile_side * slot_total * lax.axis_size("dp") * lax.axis_size("fsdp")
    )
    stacked = jnp.concatenate([weight_term, affine_fsdp], axis=0) * loss_scale
    summed = halving_doubling_sum(stacked, "dp")
    grad_conv = summed[:row_block]
    grad_affine = summed[row_block : row_block + affine.shape[0]]
    return (block_output, grad_input, grad_conv, grad_affine)


def solution(mesh):
    placed = (
        P(("dp", "fsdp"), None, None, None),
        P(("dp", "fsdp")),
        P(("dp", "fsdp"), None, None, None),
        P(("dp", "fsdp")),
        P(),
        P(),
        P(),
        P(),
        P(),
        P("fsdp", None),
        P("fsdp", None),
    )
    return jax.shard_map(
        body,
        mesh=mesh,
        in_specs=placed,
        out_specs=(
            P(("dp", "fsdp"), None, None, None),
            P(("dp", "fsdp"), None, None, None),
            P("fsdp", None),
            P(),
        ),
        check_vma=False,
    )
```

```python
import math

import jax
import jax.numpy as jnp
from jax import lax
from jax.sharding import PartitionSpec as P

GROUPS = 32
CONV_DIMS = ("NHWC", "HWIO", "NHWC")
BACK_DIMS = ("NHWC", "HWOI", "NHWC")


def group_mean(channel_sums, per_group):
    tiles, channels = channel_sums.shape
    width = channels // GROUPS
    grouped = channel_sums.reshape(tiles, GROUPS, width).sum(axis=-1) / per_group
    return jnp.repeat(grouped, width, axis=1)


def shifted(padded, tap, tile_side):
    row_off = tap // 3
    col_off = tap % 3
    return lax.dynamic_slice(
        padded,
        (0, row_off, col_off, 0),
        (padded.shape[0], tile_side, tile_side, padded.shape[3]),
    )


def halving_doubling_sum(block, axis):
    size = lax.axis_size(axis)
    levels = size.bit_length() - 1
    if size != 1 << levels or levels == 0:
        return lax.psum(block, axis)
    order = [0, levels - 1] + list(range(1, levels - 1)) if levels > 1 else [0]
    rows = block.shape[0]
    padded_rows = -(-rows // size) * size
    cur = jnp.pad(block, ((0, padded_rows - rows), (0, 0)))
    index = lax.axis_index(axis)
    for level in order:
        half = cur.shape[0] // 2
        low = ((index >> level) & 1) == 0
        send = jnp.where(low, cur[half:], cur[:half])
        keep = jnp.where(low, cur[:half], cur[half:])
        pairs = [(i, i ^ (1 << level)) for i in range(size)]
        cur = keep + lax.ppermute(send, axis, pairs)
    for level in reversed(order):
        low = ((index >> level) & 1) == 0
        pairs = [(i, i ^ (1 << level)) for i in range(size)]
        other = lax.ppermute(cur, axis, pairs)
        cur = jnp.where(low, jnp.concatenate([cur, other]), jnp.concatenate([other, cur]))
    return cur[:rows]


def doubling_sum(block, axis):
    size = lax.axis_size(axis)
    levels = size.bit_length() - 1
    if size != 1 << levels:
        return lax.psum(block, axis)
    for level in range(levels):
        pairs = [(i, i ^ (1 << level)) for i in range(size)]
        block = block + lax.ppermute(block, axis, pairs)
    return block


def body(
    latents,
    bucket,
    cotangent,
    tile_count,
    cond_table,
    norm_gain,
    norm_shift,
    conv_bias,
    down_bias,
    conv_weight,
    down_weight,
):
    slot_total, tile_side, _, channels = latents.shape
    row_block = conv_weight.shape[0]

    live = jnp.arange(slot_total, dtype=jnp.int32) < tile_count[0]
    live4 = live[:, None, None, None]
    masked_cot = jnp.where(live4, cotangent, jnp.zeros_like(cotangent))

    per_group = tile_side * tile_side * (channels // GROUPS)
    values = latents.astype(jnp.float32)
    center = group_mean(jnp.sum(values, axis=(1, 2)), per_group)
    deviation = values - center[:, None, None, :]
    spread = group_mean(jnp.sum(deviation * deviation, axis=(1, 2)), per_group)
    inv_std = lax.rsqrt(spread + 1e-05)[:, None, None, :]
    normed = deviation * inv_std
    pre_act = normed * norm_gain + norm_shift
    sigmoid_v = jax.nn.sigmoid(pre_act)
    activated = (pre_act * sigmoid_v).astype(jnp.bfloat16)
    cot_rows = masked_cot.reshape(-1, channels)
    act_rows = activated.reshape(-1, channels)
    sent = jnp.concatenate([conv_weight, down_weight, cot_rows, act_rows], axis=0)
    got = lax.all_gather(sent, "fsdp", axis=0, tiled=False)
    edges = [0]
    for part in (conv_weight, down_weight, cot_rows, act_rows):
        edges.append(edges[-1] + part.shape[0])
    pieces = [got[:, edges[i] : edges[i + 1]] for i in range(4)]
    conv_kernel = pieces[0].reshape(3, 3, channels, channels)
    down_kernel = pieces[1].reshape(3, 3, channels, channels)
    cot_all = pieces[2].reshape((-1,) + masked_cot.shape[1:])
    act_all = pieces[3].reshape((-1,) + activated.shape[1:])

    conditioning = cond_table[bucket]
    conv_out = lax.conv_general_dilated(
        activated,
        conv_kernel,
        (1, 1),
        ((1, 1), (1, 1)),
        dimension_numbers=CONV_DIMS,
        preferred_element_type=jnp.float32,
    )
    conv_out = conv_out + conv_bias + conditioning[:, None, None, :]
    residual = (values + conv_out).astype(jnp.bfloat16)
    down_out = lax.conv_general_dilated(
        residual,
        down_kernel,
        (2, 2),
        ((1, 1), (1, 1)),
        dimension_numbers=CONV_DIMS,
        preferred_element_type=jnp.float32,
    )
    block_output = (down_out + down_bias).astype(jnp.bfloat16)
    block_output = jnp.where(live4, block_output, jnp.zeros_like(block_output))

    resid_all = lax.conv_general_dilated(
        cot_all,
        down_kernel[::-1, ::-1],
        (1, 1),
        ((1, 2), (1, 2)),
        lhs_dilation=(2, 2),
        dimension_numbers=BACK_DIMS,
        preferred_element_type=jnp.float32,
    )
    hid_all = resid_all.astype(jnp.bfloat16).reshape(-1, channels)
    grad_resid = lax.dynamic_slice_in_dim(
        resid_all, lax.axis_index("fsdp") * slot_total, slot_total, axis=0
    )
    grad_hidden = grad_resid.astype(jnp.bfloat16)
    grad_act = lax.conv_general_dilated(
        grad_hidden,
        conv_kernel[::-1, ::-1],
        (1, 1),
        ((1, 1), (1, 1)),
        dimension_numbers=BACK_DIMS,
        preferred_element_type=jnp.float32,
    )
    grad_pre = grad_act * sigmoid_v * (1.0 + pre_act * (1.0 - sigmoid_v))
    scaled = grad_pre * norm_gain
    mean_one = group_mean(jnp.sum(scaled, axis=(1, 2)), per_group)[:, None, None, :]
    mean_two = group_mean(jnp.sum(scaled * normed, axis=(1, 2)), per_group)[:, None, None, :]
    grad_input = (grad_resid + inv_std * (scaled - mean_one - normed * mean_two)).astype(
        jnp.bfloat16
    )
    affine = jnp.stack(
        [
            jnp.sum(grad_pre * normed, axis=(0, 1, 2)),
            jnp.sum(grad_pre, axis=(0, 1, 2)),
            jnp.sum(grad_resid, axis=(0, 1, 2)),
        ]
    )
    affine_fsdp = doubling_sum(affine, "fsdp")

    first_row = lax.axis_index("fsdp") * row_block
    first_tap = first_row // channels
    first_chan = first_row % channels
    span = (row_block + channels - 1) // channels + 1
    act_pad = jnp.pad(act_all, ((0, 0), (1, 1), (1, 1), (0, 0)))
    taps = [
        shifted(act_pad, jnp.minimum(first_tap + extra, 8), tile_side) for extra in range(span)
    ]
    tap_cols = jnp.concatenate(taps, axis=-1)
    own_cols = lax.dynamic_slice_in_dim(tap_cols, first_chan, row_block, axis=3)
    weight_term = lax.dot_general(
        own_cols.reshape(-1, row_block),
        hid_all,
        (((0,), (0,)), ((), ())),
        preferred_element_type=jnp.float32,
    )
    loss_scale = 4.0 / math.sqrt(
        tile_side * tile_side * slot_total * lax.axis_size("dp") * lax.axis_size("fsdp")
    )
    stacked = jnp.concatenate([weight_term, affine_fsdp], axis=0) * loss_scale
    summed = halving_doubling_sum(stacked, "dp")
    grad_conv = summed[:row_block]
    grad_affine = summed[row_block : row_block + affine.shape[0]]
    return (block_output, grad_input, grad_conv, grad_affine)


def solution(mesh):
    placed = (
        P(("dp", "fsdp"), None, None, None),
        P(("dp", "fsdp")),
        P(("dp", "fsdp"), None, None, None),
        P(("dp", "fsdp")),
        P(),
        P(),
        P(),
        P(),
        P(),
        P("fsdp", None),
        P("fsdp", None),
    )
    return jax.shard_map(
        body,
        mesh=mesh,
        in_specs=placed,
        out_specs=(
            P(("dp", "fsdp"), None, None, None),
            P(("dp", "fsdp"), None, None, None),
            P("fsdp", None),
            P(),
        ),
        check_vma=False,
    )
```

```python
import math

import jax
import jax.numpy as jnp
from jax import lax
from jax.sharding import PartitionSpec as P

GROUPS = 32
CONV_DIMS = ("NHWC", "HWIO", "NHWC")
BACK_DIMS = ("NHWC", "HWOI", "NHWC")


def group_mean(channel_sums, per_group):
    tiles, channels = channel_sums.shape
    width = channels // GROUPS
    grouped = channel_sums.reshape(tiles, GROUPS, width).sum(axis=-1) / per_group
    return jnp.repeat(grouped, width, axis=1)


def shifted(padded, tap, tile_side):
    row_off = tap // 3
    col_off = tap % 3
    return lax.dynamic_slice(
        padded,
        (0, row_off, col_off, 0),
        (padded.shape[0], tile_side, tile_side, padded.shape[3]),
    )


def halving_doubling_sum(block, axis):
    size = lax.axis_size(axis)
    levels = size.bit_length() - 1
    if size != 1 << levels or levels == 0:
        return lax.psum(block, axis)
    order = [0, levels - 1] + list(range(1, levels - 1)) if levels > 1 else [0]
    rows = block.shape[0]
    padded_rows = -(-rows // size) * size
    cur = jnp.pad(block, ((0, padded_rows - rows), (0, 0)))
    index = lax.axis_index(axis)
    for level in order:
        half = cur.shape[0] // 2
        low = ((index >> level) & 1) == 0
        send = jnp.where(low, cur[half:], cur[:half])
        keep = jnp.where(low, cur[:half], cur[half:])
        pairs = [(i, i ^ (1 << level)) for i in range(size)]
        cur = keep + lax.ppermute(send, axis, pairs)
    for level in reversed(order):
        low = ((index >> level) & 1) == 0
        pairs = [(i, i ^ (1 << level)) for i in range(size)]
        other = lax.ppermute(cur, axis, pairs)
        cur = jnp.where(low, jnp.concatenate([cur, other]), jnp.concatenate([other, cur]))
    return cur[:rows]


def doubling_sum(block, axis):
    size = lax.axis_size(axis)
    levels = size.bit_length() - 1
    if size != 1 << levels:
        return lax.psum(block, axis)
    for level in range(levels):
        pairs = [(i, i ^ (1 << level)) for i in range(size)]
        block = block + lax.ppermute(block, axis, pairs)
    return block


def body(
    latents,
    bucket,
    cotangent,
    tile_count,
    cond_table,
    norm_gain,
    norm_shift,
    conv_bias,
    down_bias,
    conv_weight,
    down_weight,
):
    slot_total, tile_side, _, channels = latents.shape
    row_block = conv_weight.shape[0]

    live = jnp.arange(slot_total, dtype=jnp.int32) < tile_count[0]
    live4 = live[:, None, None, None]
    masked_cot = jnp.where(live4, cotangent, jnp.zeros_like(cotangent))

    per_group = tile_side * tile_side * (channels // GROUPS)
    values = latents.astype(jnp.float32)
    center = group_mean(jnp.sum(values, axis=(1, 2)), per_group)
    deviation = values - center[:, None, None, :]
    spread = group_mean(jnp.sum(deviation * deviation, axis=(1, 2)), per_group)
    inv_std = lax.rsqrt(spread + 1e-05)[:, None, None, :]
    normed = deviation * inv_std
    pre_act = normed * norm_gain + norm_shift
    sigmoid_v = jax.nn.sigmoid(pre_act)
    activated = (pre_act * sigmoid_v).astype(jnp.bfloat16)
    cot_rows = masked_cot.reshape(-1, channels)
    act_rows = activated.reshape(-1, channels)
    sent = jnp.concatenate([conv_weight, down_weight, cot_rows, act_rows], axis=0)
    got = lax.all_gather(sent, "fsdp", axis=0, tiled=False)
    edges = [0]
    for part in (conv_weight, down_weight, cot_rows, act_rows):
        edges.append(edges[-1] + part.shape[0])
    pieces = [got[:, edges[i] : edges[i + 1]] for i in range(4)]
    conv_kernel = pieces[0].reshape(3, 3, channels, channels)
    down_kernel = pieces[1].reshape(3, 3, channels, channels)
    cot_all = pieces[2].reshape((-1,) + masked_cot.shape[1:])
    act_all = pieces[3].reshape((-1,) + activated.shape[1:])

    conditioning = cond_table[bucket]
    conv_out = lax.conv_general_dilated(
        activated,
        conv_kernel,
        (1, 1),
        ((1, 1), (1, 1)),
        dimension_numbers=CONV_DIMS,
        preferred_element_type=jnp.float32,
    )
    conv_out = conv_out + conv_bias + conditioning[:, None, None, :]
    residual = (values + conv_out).astype(jnp.bfloat16)
    down_out = lax.conv_general_dilated(
        residual,
        down_kernel,
        (2, 2),
        ((1, 1), (1, 1)),
        dimension_numbers=CONV_DIMS,
        preferred_element_type=jnp.float32,
    )
    block_output = (down_out + down_bias).astype(jnp.bfloat16)
    block_output = jnp.where(live4, block_output, jnp.zeros_like(block_output))

    resid_all = lax.conv_general_dilated(
        cot_all,
        down_kernel[::-1, ::-1],
        (1, 1),
        ((1, 2), (1, 2)),
        lhs_dilation=(2, 2),
        dimension_numbers=BACK_DIMS,
        preferred_element_type=jnp.float32,
    )
    hid_all = resid_all.astype(jnp.bfloat16).reshape(-1, channels)
    grad_resid = lax.dynamic_slice_in_dim(
        resid_all, lax.axis_index("fsdp") * slot_total, slot_total, axis=0
    )
    grad_hidden = grad_resid.astype(jnp.bfloat16)
    grad_act = lax.conv_general_dilated(
        grad_hidden,
        conv_kernel[::-1, ::-1],
        (1, 1),
        ((1, 1), (1, 1)),
        dimension_numbers=BACK_DIMS,
        preferred_element_type=jnp.float32,
    )
    grad_pre = grad_act * sigmoid_v * (1.0 + pre_act * (1.0 - sigmoid_v))
    scaled = grad_pre * norm_gain
    mean_one = group_mean(jnp.sum(scaled, axis=(1, 2)), per_group)[:, None, None, :]
    mean_two = group_mean(jnp.sum(scaled * normed, axis=(1, 2)), per_group)[:, None, None, :]
    grad_input = (grad_resid + inv_std * (scaled - mean_one - normed * mean_two)).astype(
        jnp.bfloat16
    )
    affine = jnp.stack(
        [
            jnp.sum(grad_pre * normed, axis=(0, 1, 2)),
            jnp.sum(grad_pre, axis=(0, 1, 2)),
            jnp.sum(grad_resid, axis=(0, 1, 2)),
        ]
    )

    first_row = lax.axis_index("fsdp") * row_block
    first_tap = first_row // channels
    first_chan = first_row % channels
    span = (row_block + channels - 1) // channels + 1
    act_pad = jnp.pad(act_all, ((0, 0), (1, 1), (1, 1), (0, 0)))
    taps = [
        shifted(act_pad, jnp.minimum(first_tap + extra, 8), tile_side) for extra in range(span)
    ]
    tap_cols = jnp.concatenate(taps, axis=-1)
    own_cols = lax.dynamic_slice_in_dim(tap_cols, first_chan, row_block, axis=3)
    weight_term = lax.dot_general(
        own_cols.reshape(-1, row_block),
        hid_all,
        (((0,), (0,)), ((), ())),
        preferred_element_type=jnp.float32,
    )
    loss_scale = 4.0 / math.sqrt(
        tile_side * tile_side * slot_total * lax.axis_size("dp") * lax.axis_size("fsdp")
    )
    grad_conv = halving_doubling_sum(weight_term * loss_scale, "dp")
    grad_affine = doubling_sum(doubling_sum(affine * loss_scale, "fsdp"), "dp")
    return (block_output, grad_input, grad_conv, grad_affine)


def solution(mesh):
    placed = (
        P(("dp", "fsdp"), None, None, None),
        P(("dp", "fsdp")),
        P(("dp", "fsdp"), None, None, None),
        P(("dp", "fsdp")),
        P(),
        P(),
        P(),
        P(),
        P(),
        P("fsdp", None),
        P("fsdp", None),
    )
    return jax.shard_map(
        body,
        mesh=mesh,
        in_specs=placed,
        out_specs=(
            P(("dp", "fsdp"), None, None, None),
            P(("dp", "fsdp"), None, None, None),
            P("fsdp", None),
            P(),
        ),
        check_vma=False,
    )
```

```python
import math

import jax
import jax.numpy as jnp
from jax import lax
from jax.sharding import PartitionSpec as P

GROUPS = 32
CONV_DIMS = ("NHWC", "HWIO", "NHWC")
BACK_DIMS = ("NHWC", "HWOI", "NHWC")


def group_mean(channel_sums, per_group):
    tiles, channels = channel_sums.shape
    width = channels // GROUPS
    grouped = channel_sums.reshape(tiles, GROUPS, width).sum(axis=-1) / per_group
    return jnp.repeat(grouped, width, axis=1)


def shifted(padded, tap, tile_side):
    row_off = tap // 3
    col_off = tap % 3
    return lax.dynamic_slice(
        padded,
        (0, row_off, col_off, 0),
        (padded.shape[0], tile_side, tile_side, padded.shape[3]),
    )


def halving_doubling_sum(block, axis, side):
    size = lax.axis_size(axis)
    levels = size.bit_length() - 1
    if size != 1 << levels or levels == 0:
        return lax.psum(block, axis), side
    order = [0, levels - 1] + list(range(1, levels - 1)) if levels > 1 else [0]
    rows = block.shape[0]
    padded_rows = -(-rows // size) * size
    cur = jnp.pad(block, ((0, padded_rows - rows), (0, 0)))
    index = lax.axis_index(axis)
    for level in order:
        half = cur.shape[0] // 2
        low = ((index >> level) & 1) == 0
        send = jnp.where(low, cur[half:], cur[:half])
        keep = jnp.where(low, cur[:half], cur[half:])
        pairs = [(i, i ^ (1 << level)) for i in range(size)]
        cur = keep + lax.ppermute(send, axis, pairs)
        if level == order[0]:
            cur, side = lax.optimization_barrier((cur, side))
    for level in reversed(order):
        low = ((index >> level) & 1) == 0
        pairs = [(i, i ^ (1 << level)) for i in range(size)]
        other = lax.ppermute(cur, axis, pairs)
        cur = jnp.where(low, jnp.concatenate([cur, other]), jnp.concatenate([other, cur]))
    return cur[:rows], side


def doubling_sum(block, axis):
    size = lax.axis_size(axis)
    levels = size.bit_length() - 1
    if size != 1 << levels:
        return lax.psum(block, axis)
    for level in range(levels):
        pairs = [(i, i ^ (1 << level)) for i in range(size)]
        block = block + lax.ppermute(block, axis, pairs)
    return block


def body(
    latents,
    bucket,
    cotangent,
    tile_count,
    cond_table,
    norm_gain,
    norm_shift,
    conv_bias,
    down_bias,
    conv_weight,
    down_weight,
):
    slot_total, tile_side, _, channels = latents.shape
    row_block = conv_weight.shape[0]

    live = jnp.arange(slot_total, dtype=jnp.int32) < tile_count[0]
    live4 = live[:, None, None, None]
    masked_cot = jnp.where(live4, cotangent, jnp.zeros_like(cotangent))

    per_group = tile_side * tile_side * (channels // GROUPS)
    values = latents.astype(jnp.float32)
    center = group_mean(jnp.sum(values, axis=(1, 2)), per_group)
    deviation = values - center[:, None, None, :]
    spread = group_mean(jnp.sum(deviation * deviation, axis=(1, 2)), per_group)
    inv_std = lax.rsqrt(spread + 1e-05)[:, None, None, :]
    normed = deviation * inv_std
    pre_act = normed * norm_gain + norm_shift
    sigmoid_v = jax.nn.sigmoid(pre_act)
    activated = (pre_act * sigmoid_v).astype(jnp.bfloat16)
    cot_rows = masked_cot.reshape(-1, channels)
    act_rows = activated.reshape(-1, channels)
    sent = jnp.concatenate([conv_weight, down_weight, cot_rows, act_rows], axis=0)
    got = lax.all_gather(sent, "fsdp", axis=0, tiled=False)
    edges = [0]
    for part in (conv_weight, down_weight, cot_rows, act_rows):
        edges.append(edges[-1] + part.shape[0])
    pieces = [got[:, edges[i] : edges[i + 1]] for i in range(4)]
    conv_kernel = pieces[0].reshape(3, 3, channels, channels)
    down_kernel = pieces[1].reshape(3, 3, channels, channels)
    cot_all = pieces[2].reshape((-1,) + masked_cot.shape[1:])
    act_all = pieces[3].reshape((-1,) + activated.shape[1:])

    conditioning = cond_table[bucket]
    conv_out = lax.conv_general_dilated(
        activated,
        conv_kernel,
        (1, 1),
        ((1, 1), (1, 1)),
        dimension_numbers=CONV_DIMS,
        preferred_element_type=jnp.float32,
    )
    conv_out = conv_out + conv_bias + conditioning[:, None, None, :]
    residual = (values + conv_out).astype(jnp.bfloat16)
    down_out = lax.conv_general_dilated(
        residual,
        down_kernel,
        (2, 2),
        ((1, 1), (1, 1)),
        dimension_numbers=CONV_DIMS,
        preferred_element_type=jnp.float32,
    )
    block_output = (down_out + down_bias).astype(jnp.bfloat16)
    block_output = jnp.where(live4, block_output, jnp.zeros_like(block_output))

    resid_all = lax.conv_general_dilated(
        cot_all,
        down_kernel[::-1, ::-1],
        (1, 1),
        ((1, 2), (1, 2)),
        lhs_dilation=(2, 2),
        dimension_numbers=BACK_DIMS,
        preferred_element_type=jnp.float32,
    )
    hid_all = resid_all.astype(jnp.bfloat16).reshape(-1, channels)
    grad_resid = lax.dynamic_slice_in_dim(
        resid_all, lax.axis_index("fsdp") * slot_total, slot_total, axis=0
    )
    grad_hidden = grad_resid.astype(jnp.bfloat16)
    grad_act = lax.conv_general_dilated(
        grad_hidden,
        conv_kernel[::-1, ::-1],
        (1, 1),
        ((1, 1), (1, 1)),
        dimension_numbers=BACK_DIMS,
        preferred_element_type=jnp.float32,
    )
    grad_pre = grad_act * sigmoid_v * (1.0 + pre_act * (1.0 - sigmoid_v))
    scaled = grad_pre * norm_gain
    mean_one = group_mean(jnp.sum(scaled, axis=(1, 2)), per_group)[:, None, None, :]
    mean_two = group_mean(jnp.sum(scaled * normed, axis=(1, 2)), per_group)[:, None, None, :]
    grad_input = (grad_resid + inv_std * (scaled - mean_one - normed * mean_two)).astype(
        jnp.bfloat16
    )
    affine = jnp.stack(
        [
            jnp.sum(grad_pre * normed, axis=(0, 1, 2)),
            jnp.sum(grad_pre, axis=(0, 1, 2)),
            jnp.sum(grad_resid, axis=(0, 1, 2)),
        ]
    )
    affine_fsdp = doubling_sum(affine, "fsdp")

    first_row = lax.axis_index("fsdp") * row_block
    first_tap = first_row // channels
    first_chan = first_row % channels
    span = (row_block + channels - 1) // channels + 1
    act_flat = act_all.reshape(-1, channels)
    hid_pad = jnp.pad(hid_all.reshape(act_all.shape), ((0, 0), (1, 1), (1, 1), (0, 0)))
    tap_terms = []
    for extra in range(span):
        tap = jnp.minimum(first_tap + extra, 8)
        hid_shift = shifted(hid_pad, 8 - tap, tile_side)
        tap_terms.append(
            lax.dot_general(
                act_flat,
                hid_shift.reshape(-1, channels),
                (((0,), (0,)), ((), ())),
                preferred_element_type=jnp.float32,
            )
        )
    weight_term = lax.dynamic_slice_in_dim(
        jnp.concatenate(tap_terms, axis=0), first_chan, row_block, axis=0
    )
    loss_scale = 4.0 / math.sqrt(
        tile_side * tile_side * slot_total * lax.axis_size("dp") * lax.axis_size("fsdp")
    )
    stacked = jnp.concatenate([weight_term, affine_fsdp], axis=0) * loss_scale
    summed, (block_output, grad_input) = halving_doubling_sum(
        stacked, "dp", (block_output, grad_input)
    )
    grad_conv = summed[:row_block]
    grad_affine = summed[row_block : row_block + affine.shape[0]]
    return (block_output, grad_input, grad_conv, grad_affine)


def solution(mesh):
    placed = (
        P(("dp", "fsdp"), None, None, None),
        P(("dp", "fsdp")),
        P(("dp", "fsdp"), None, None, None),
        P(("dp", "fsdp")),
        P(),
        P(),
        P(),
        P(),
        P(),
        P("fsdp", None),
        P("fsdp", None),
    )
    return jax.shard_map(
        body,
        mesh=mesh,
        in_specs=placed,
        out_specs=(
            P(("dp", "fsdp"), None, None, None),
            P(("dp", "fsdp"), None, None, None),
            P("fsdp", None),
            P(),
        ),
        check_vma=False,
    )
```

```python
import math

import jax
import jax.numpy as jnp
from jax import lax
from jax.sharding import PartitionSpec as P

GROUPS = 32
CONV_DIMS = ("NHWC", "HWIO", "NHWC")
BACK_DIMS = ("NHWC", "HWOI", "NHWC")


def group_mean(channel_sums, per_group):
    tiles, channels = channel_sums.shape
    width = channels // GROUPS
    grouped = channel_sums.reshape(tiles, GROUPS, width).sum(axis=-1) / per_group
    return jnp.repeat(grouped, width, axis=1)


def shifted(padded, tap, tile_side):
    row_off = tap // 3
    col_off = tap % 3
    return lax.dynamic_slice(
        padded,
        (0, row_off, col_off, 0),
        (padded.shape[0], tile_side, tile_side, padded.shape[3]),
    )


def halving_doubling_sum(block, axis):
    size = lax.axis_size(axis)
    levels = size.bit_length() - 1
    if size != 1 << levels or levels == 0:
        return lax.psum(block, axis)
    order = [0, levels - 1] + list(range(1, levels - 1)) if levels > 1 else [0]
    rows = block.shape[0]
    padded_rows = -(-rows // size) * size
    cur = jnp.pad(block, ((0, padded_rows - rows), (0, 0)))
    index = lax.axis_index(axis)
    for level in order:
        half = cur.shape[0] // 2
        low = ((index >> level) & 1) == 0
        send = jnp.where(low, cur[half:], cur[:half])
        keep = jnp.where(low, cur[:half], cur[half:])
        pairs = [(i, i ^ (1 << level)) for i in range(size)]
        cur = keep + lax.ppermute(send, axis, pairs)
    for level in reversed(order):
        low = ((index >> level) & 1) == 0
        pairs = [(i, i ^ (1 << level)) for i in range(size)]
        other = lax.ppermute(cur, axis, pairs)
        cur = jnp.where(low, jnp.concatenate([cur, other]), jnp.concatenate([other, cur]))
    return cur[:rows]


def doubling_sum(block, axis):
    size = lax.axis_size(axis)
    levels = size.bit_length() - 1
    if size != 1 << levels:
        return lax.psum(block, axis)
    for level in range(levels):
        pairs = [(i, i ^ (1 << level)) for i in range(size)]
        block = block + lax.ppermute(block, axis, pairs)
    return block


def body(
    latents,
    bucket,
    cotangent,
    tile_count,
    cond_table,
    norm_gain,
    norm_shift,
    conv_bias,
    down_bias,
    conv_weight,
    down_weight,
):
    slot_total, tile_side, _, channels = latents.shape
    row_block = conv_weight.shape[0]

    live = jnp.arange(slot_total, dtype=jnp.int32) < tile_count[0]
    live4 = live[:, None, None, None]
    masked_cot = jnp.where(live4, cotangent, jnp.zeros_like(cotangent))

    per_group = tile_side * tile_side * (channels // GROUPS)
    values = latents.astype(jnp.float32)
    center = group_mean(jnp.sum(values, axis=(1, 2)), per_group)
    deviation = values - center[:, None, None, :]
    spread = group_mean(jnp.sum(deviation * deviation, axis=(1, 2)), per_group)
    inv_std = lax.rsqrt(spread + 1e-05)[:, None, None, :]
    normed = deviation * inv_std
    pre_act = normed * norm_gain + norm_shift
    sigmoid_v = jax.nn.sigmoid(pre_act)
    activated = (pre_act * sigmoid_v).astype(jnp.bfloat16)
    cot_rows = masked_cot.reshape(-1, channels)
    act_rows = activated.reshape(-1, channels)
    first_parts = (down_weight, cot_rows, act_rows)
    got = lax.all_gather(jnp.concatenate(first_parts, axis=0), "fsdp", axis=0, tiled=False)
    edges = [0]
    for part in first_parts:
        edges.append(edges[-1] + part.shape[0])
    pieces = [got[:, edges[i] : edges[i + 1]] for i in range(len(first_parts))]
    down_kernel = pieces[0].reshape(3, 3, channels, channels)
    cot_all = pieces[1].reshape((-1,) + masked_cot.shape[1:])
    act_all = pieces[2].reshape((-1,) + activated.shape[1:])
    conv_shard, _ = lax.optimization_barrier((conv_weight, got))
    conv_kernel = lax.all_gather(conv_shard, "fsdp", axis=0, tiled=True).reshape(
        3, 3, channels, channels
    )

    conditioning = cond_table[bucket]
    conv_out = lax.conv_general_dilated(
        activated,
        conv_kernel,
        (1, 1),
        ((1, 1), (1, 1)),
        dimension_numbers=CONV_DIMS,
        preferred_element_type=jnp.float32,
    )
    conv_out = conv_out + conv_bias + conditioning[:, None, None, :]
    residual = (values + conv_out).astype(jnp.bfloat16)
    down_out = lax.conv_general_dilated(
        residual,
        down_kernel,
        (2, 2),
        ((1, 1), (1, 1)),
        dimension_numbers=CONV_DIMS,
        preferred_element_type=jnp.float32,
    )
    block_output = (down_out + down_bias).astype(jnp.bfloat16)
    block_output = jnp.where(live4, block_output, jnp.zeros_like(block_output))

    resid_all = lax.conv_general_dilated(
        cot_all,
        down_kernel[::-1, ::-1],
        (1, 1),
        ((1, 2), (1, 2)),
        lhs_dilation=(2, 2),
        dimension_numbers=BACK_DIMS,
        preferred_element_type=jnp.float32,
    )
    hid_all = resid_all.astype(jnp.bfloat16).reshape(-1, channels)
    grad_resid = lax.dynamic_slice_in_dim(
        resid_all, lax.axis_index("fsdp") * slot_total, slot_total, axis=0
    )
    grad_hidden = grad_resid.astype(jnp.bfloat16)
    grad_act = lax.conv_general_dilated(
        grad_hidden,
        conv_kernel[::-1, ::-1],
        (1, 1),
        ((1, 1), (1, 1)),
        dimension_numbers=BACK_DIMS,
        preferred_element_type=jnp.float32,
    )
    grad_pre = grad_act * sigmoid_v * (1.0 + pre_act * (1.0 - sigmoid_v))
    scaled = grad_pre * norm_gain
    mean_one = group_mean(jnp.sum(scaled, axis=(1, 2)), per_group)[:, None, None, :]
    mean_two = group_mean(jnp.sum(scaled * normed, axis=(1, 2)), per_group)[:, None, None, :]
    grad_input = (grad_resid + inv_std * (scaled - mean_one - normed * mean_two)).astype(
        jnp.bfloat16
    )
    affine = jnp.stack(
        [
            jnp.sum(grad_pre * normed, axis=(0, 1, 2)),
            jnp.sum(grad_pre, axis=(0, 1, 2)),
            jnp.sum(grad_resid, axis=(0, 1, 2)),
        ]
    )

    first_row = lax.axis_index("fsdp") * row_block
    first_tap = first_row // channels
    first_chan = first_row % channels
    span = (row_block + channels - 1) // channels + 1
    act_pad = jnp.pad(act_all, ((0, 0), (1, 1), (1, 1), (0, 0)))
    taps = [
        shifted(act_pad, jnp.minimum(first_tap + extra, 8), tile_side) for extra in range(span)
    ]
    tap_cols = jnp.concatenate(taps, axis=-1)
    own_cols = lax.dynamic_slice_in_dim(tap_cols, first_chan, row_block, axis=3)
    weight_term = lax.dot_general(
        own_cols.reshape(-1, row_block),
        hid_all,
        (((0,), (0,)), ((), ())),
        preferred_element_type=jnp.float32,
    )
    loss_scale = 4.0 / math.sqrt(
        tile_side * tile_side * slot_total * lax.axis_size("dp") * lax.axis_size("fsdp")
    )
    grad_conv = halving_doubling_sum(weight_term * loss_scale, "dp")
    grad_affine = doubling_sum(doubling_sum(affine * loss_scale, "fsdp"), "dp")
    return (block_output, grad_input, grad_conv, grad_affine)


def solution(mesh):
    placed = (
        P(("dp", "fsdp"), None, None, None),
        P(("dp", "fsdp")),
        P(("dp", "fsdp"), None, None, None),
        P(("dp", "fsdp")),
        P(),
        P(),
        P(),
        P(),
        P(),
        P("fsdp", None),
        P("fsdp", None),
    )
    return jax.shard_map(
        body,
        mesh=mesh,
        in_specs=placed,
        out_specs=(
            P(("dp", "fsdp"), None, None, None),
            P(("dp", "fsdp"), None, None, None),
            P("fsdp", None),
            P(),
        ),
        check_vma=False,
    )
```

```python
import math

import jax
import jax.numpy as jnp
from jax import lax
from jax.sharding import PartitionSpec as P

GROUPS = 32
CONV_DIMS = ("NHWC", "HWIO", "NHWC")
BACK_DIMS = ("NHWC", "HWOI", "NHWC")


def group_mean(channel_sums, per_group):
    tiles, channels = channel_sums.shape
    width = channels // GROUPS
    grouped = channel_sums.reshape(tiles, GROUPS, width).sum(axis=-1) / per_group
    return jnp.repeat(grouped, width, axis=1)


def shifted(padded, tap, tile_side):
    row_off = tap // 3
    col_off = tap % 3
    return lax.dynamic_slice(
        padded,
        (0, row_off, col_off, 0),
        (padded.shape[0], tile_side, tile_side, padded.shape[3]),
    )


def halving_doubling_sum(block, axis, side, tie_step):
    size = lax.axis_size(axis)
    levels = size.bit_length() - 1
    if size != 1 << levels or levels == 0:
        return lax.psum(block, axis), side
    order = [0, levels - 1] + list(range(1, levels - 1)) if levels > 1 else [0]
    rows = block.shape[0]
    padded_rows = -(-rows // size) * size
    cur = jnp.pad(block, ((0, padded_rows - rows), (0, 0)))
    index = lax.axis_index(axis)
    for step, level in enumerate(order):
        if step == tie_step:
            cur, side = lax.optimization_barrier((cur, side))
        half = cur.shape[0] // 2
        low = ((index >> level) & 1) == 0
        send = jnp.where(low, cur[half:], cur[:half])
        keep = jnp.where(low, cur[:half], cur[half:])
        pairs = [(i, i ^ (1 << level)) for i in range(size)]
        cur = keep + lax.ppermute(send, axis, pairs)
    for level in reversed(order):
        low = ((index >> level) & 1) == 0
        pairs = [(i, i ^ (1 << level)) for i in range(size)]
        other = lax.ppermute(cur, axis, pairs)
        cur = jnp.where(low, jnp.concatenate([cur, other]), jnp.concatenate([other, cur]))
    return cur[:rows], side


def doubling_sum(block, axis, side=None, tie_step=-1):
    size = lax.axis_size(axis)
    levels = size.bit_length() - 1
    if size != 1 << levels:
        return lax.psum(block, axis), side
    for level in range(levels):
        if level == tie_step:
            block, side = lax.optimization_barrier((block, side))
        pairs = [(i, i ^ (1 << level)) for i in range(size)]
        block = block + lax.ppermute(block, axis, pairs)
    return block, side


def body(
    latents,
    bucket,
    cotangent,
    tile_count,
    cond_table,
    norm_gain,
    norm_shift,
    conv_bias,
    down_bias,
    conv_weight,
    down_weight,
):
    slot_total, tile_side, _, channels = latents.shape
    row_block = conv_weight.shape[0]

    live = jnp.arange(slot_total, dtype=jnp.int32) < tile_count[0]
    live4 = live[:, None, None, None]
    masked_cot = jnp.where(live4, cotangent, jnp.zeros_like(cotangent))

    per_group = tile_side * tile_side * (channels // GROUPS)
    values = latents.astype(jnp.float32)
    center = group_mean(jnp.sum(values, axis=(1, 2)), per_group)
    deviation = values - center[:, None, None, :]
    spread = group_mean(jnp.sum(deviation * deviation, axis=(1, 2)), per_group)
    inv_std = lax.rsqrt(spread + 1e-05)[:, None, None, :]
    normed = deviation * inv_std
    pre_act = normed * norm_gain + norm_shift
    sigmoid_v = jax.nn.sigmoid(pre_act)
    activated = (pre_act * sigmoid_v).astype(jnp.bfloat16)
    cot_rows = masked_cot.reshape(-1, channels)
    act_rows = activated.reshape(-1, channels)
    first_parts = (down_weight, cot_rows, act_rows)
    got = lax.all_gather(jnp.concatenate(first_parts, axis=0), "fsdp", axis=0, tiled=False)
    edges = [0]
    for part in first_parts:
        edges.append(edges[-1] + part.shape[0])
    pieces = [got[:, edges[i] : edges[i + 1]] for i in range(len(first_parts))]
    down_kernel = pieces[0].reshape(3, 3, channels, channels)
    cot_all = pieces[1].reshape((-1,) + masked_cot.shape[1:])
    act_all = pieces[2].reshape((-1,) + activated.shape[1:])
    conv_shard, _ = lax.optimization_barrier((conv_weight, got))
    conv_kernel = lax.all_gather(conv_shard, "fsdp", axis=0, tiled=True).reshape(
        3, 3, channels, channels
    )

    conditioning = cond_table[bucket]
    conv_out = lax.conv_general_dilated(
        activated,
        conv_kernel,
        (1, 1),
        ((1, 1), (1, 1)),
        dimension_numbers=CONV_DIMS,
        preferred_element_type=jnp.float32,
    )
    conv_out = conv_out + conv_bias + conditioning[:, None, None, :]
    residual = (values + conv_out).astype(jnp.bfloat16)
    down_out = lax.conv_general_dilated(
        residual,
        down_kernel,
        (2, 2),
        ((1, 1), (1, 1)),
        dimension_numbers=CONV_DIMS,
        preferred_element_type=jnp.float32,
    )
    block_output = (down_out + down_bias).astype(jnp.bfloat16)
    block_output = jnp.where(live4, block_output, jnp.zeros_like(block_output))

    resid_all = lax.conv_general_dilated(
        cot_all,
        down_kernel[::-1, ::-1],
        (1, 1),
        ((1, 2), (1, 2)),
        lhs_dilation=(2, 2),
        dimension_numbers=BACK_DIMS,
        preferred_element_type=jnp.float32,
    )
    hid_all = resid_all.astype(jnp.bfloat16).reshape(-1, channels)
    grad_resid = lax.dynamic_slice_in_dim(
        resid_all, lax.axis_index("fsdp") * slot_total, slot_total, axis=0
    )
    grad_hidden = grad_resid.astype(jnp.bfloat16)
    grad_act = lax.conv_general_dilated(
        grad_hidden,
        conv_kernel[::-1, ::-1],
        (1, 1),
        ((1, 1), (1, 1)),
        dimension_numbers=BACK_DIMS,
        preferred_element_type=jnp.float32,
    )
    grad_pre = grad_act * sigmoid_v * (1.0 + pre_act * (1.0 - sigmoid_v))
    scaled = grad_pre * norm_gain
    mean_one = group_mean(jnp.sum(scaled, axis=(1, 2)), per_group)[:, None, None, :]
    mean_two = group_mean(jnp.sum(scaled * normed, axis=(1, 2)), per_group)[:, None, None, :]
    grad_input = (grad_resid + inv_std * (scaled - mean_one - normed * mean_two)).astype(
        jnp.bfloat16
    )
    affine = jnp.stack(
        [
            jnp.sum(grad_pre * normed, axis=(0, 1, 2)),
            jnp.sum(grad_pre, axis=(0, 1, 2)),
            jnp.sum(grad_resid, axis=(0, 1, 2)),
        ]
    )

    first_row = lax.axis_index("fsdp") * row_block
    first_tap = first_row // channels
    first_chan = first_row % channels
    span = (row_block + channels - 1) // channels + 1
    act_pad = jnp.pad(act_all, ((0, 0), (1, 1), (1, 1), (0, 0)))
    taps = [
        shifted(act_pad, jnp.minimum(first_tap + extra, 8), tile_side) for extra in range(span)
    ]
    tap_cols = jnp.concatenate(taps, axis=-1)
    own_cols = lax.dynamic_slice_in_dim(tap_cols, first_chan, row_block, axis=3)
    weight_term = lax.dot_general(
        own_cols.reshape(-1, row_block),
        hid_all,
        (((0,), (0,)), ((), ())),
        preferred_element_type=jnp.float32,
    )
    loss_scale = 4.0 / math.sqrt(
        tile_side * tile_side * slot_total * lax.axis_size("dp") * lax.axis_size("fsdp")
    )
    grad_conv, affine = halving_doubling_sum(weight_term * loss_scale, "dp", affine, 2)
    affine_fsdp, (block_output, grad_input) = doubling_sum(
        affine * loss_scale, "fsdp", (block_output, grad_input), 1
    )
    grad_affine, _ = doubling_sum(affine_fsdp, "dp")
    return (block_output, grad_input, grad_conv, grad_affine)


def solution(mesh):
    placed = (
        P(("dp", "fsdp"), None, None, None),
        P(("dp", "fsdp")),
        P(("dp", "fsdp"), None, None, None),
        P(("dp", "fsdp")),
        P(),
        P(),
        P(),
        P(),
        P(),
        P("fsdp", None),
        P("fsdp", None),
    )
    return jax.shard_map(
        body,
        mesh=mesh,
        in_specs=placed,
        out_specs=(
            P(("dp", "fsdp"), None, None, None),
            P(("dp", "fsdp"), None, None, None),
            P("fsdp", None),
            P(),
        ),
        check_vma=False,
    )
```

```python
import math

import jax
import jax.numpy as jnp
from jax import lax
from jax.sharding import PartitionSpec as P

GROUPS = 32
CONV_DIMS = ("NHWC", "HWIO", "NHWC")
BACK_DIMS = ("NHWC", "HWOI", "NHWC")


def group_mean(channel_sums, per_group):
    tiles, channels = channel_sums.shape
    width = channels // GROUPS
    grouped = channel_sums.reshape(tiles, GROUPS, width).sum(axis=-1) / per_group
    return jnp.repeat(grouped, width, axis=1)


def shifted(padded, tap, tile_side):
    row_off = tap // 3
    col_off = tap % 3
    return lax.dynamic_slice(
        padded,
        (0, row_off, col_off, 0),
        (padded.shape[0], tile_side, tile_side, padded.shape[3]),
    )


def halving_doubling_sum(block, axis):
    size = lax.axis_size(axis)
    levels = size.bit_length() - 1
    if size != 1 << levels or levels == 0:
        return lax.psum(block, axis)
    order = [0, levels - 1] + list(range(1, levels - 1)) if levels > 1 else [0]
    rows = block.shape[0]
    padded_rows = -(-rows // size) * size
    cur = jnp.pad(block, ((0, padded_rows - rows), (0, 0)))
    index = lax.axis_index(axis)
    for level in order:
        half = cur.shape[0] // 2
        low = ((index >> level) & 1) == 0
        send = jnp.where(low, cur[half:], cur[:half])
        keep = jnp.where(low, cur[:half], cur[half:])
        pairs = [(i, i ^ (1 << level)) for i in range(size)]
        cur = keep + lax.ppermute(send, axis, pairs)
    for level in reversed(order):
        low = ((index >> level) & 1) == 0
        pairs = [(i, i ^ (1 << level)) for i in range(size)]
        other = lax.ppermute(cur, axis, pairs)
        cur = jnp.where(low, jnp.concatenate([cur, other]), jnp.concatenate([other, cur]))
    return cur[:rows]


def doubling_sum(block, axis):
    size = lax.axis_size(axis)
    levels = size.bit_length() - 1
    if size != 1 << levels:
        return lax.psum(block, axis)
    for level in range(levels):
        pairs = [(i, i ^ (1 << level)) for i in range(size)]
        block = block + lax.ppermute(block, axis, pairs)
    return block


def exchange_sum(block, axis):
    size = lax.axis_size(axis)
    rows = block.shape[0]
    padded_rows = -(-rows // size) * size
    parts = jnp.pad(block, ((0, padded_rows - rows), (0, 0))).reshape(size, padded_rows // size, -1)
    mine = lax.all_to_all(parts, axis, 0, 0, tiled=False).sum(axis=0)
    spread = jnp.broadcast_to(mine[None], (size,) + mine.shape)
    full = lax.all_to_all(spread, axis, 0, 0, tiled=False)
    return full.reshape(padded_rows, -1)[:rows]


def gathered_sum(block, axis):
    size = lax.axis_size(axis)
    spread = jnp.broadcast_to(block[None], (size,) + block.shape)
    return lax.all_to_all(spread, axis, 0, 0, tiled=False).sum(axis=0)


def body(
    latents,
    bucket,
    cotangent,
    tile_count,
    cond_table,
    norm_gain,
    norm_shift,
    conv_bias,
    down_bias,
    conv_weight,
    down_weight,
):
    slot_total, tile_side, _, channels = latents.shape
    row_block = conv_weight.shape[0]

    live = jnp.arange(slot_total, dtype=jnp.int32) < tile_count[0]
    live4 = live[:, None, None, None]
    masked_cot = jnp.where(live4, cotangent, jnp.zeros_like(cotangent))

    per_group = tile_side * tile_side * (channels // GROUPS)
    values = latents.astype(jnp.float32)
    center = group_mean(jnp.sum(values, axis=(1, 2)), per_group)
    deviation = values - center[:, None, None, :]
    spread = group_mean(jnp.sum(deviation * deviation, axis=(1, 2)), per_group)
    inv_std = lax.rsqrt(spread + 1e-05)[:, None, None, :]
    normed = deviation * inv_std
    pre_act = normed * norm_gain + norm_shift
    sigmoid_v = jax.nn.sigmoid(pre_act)
    activated = (pre_act * sigmoid_v).astype(jnp.bfloat16)
    cot_rows = masked_cot.reshape(-1, channels)
    act_rows = activated.reshape(-1, channels)
    first_parts = (down_weight, cot_rows, act_rows)
    got = lax.all_gather(jnp.concatenate(first_parts, axis=0), "fsdp", axis=0, tiled=False)
    edges = [0]
    for part in first_parts:
        edges.append(edges[-1] + part.shape[0])
    pieces = [got[:, edges[i] : edges[i + 1]] for i in range(len(first_parts))]
    down_kernel = pieces[0].reshape(3, 3, channels, channels)
    cot_all = pieces[1].reshape((-1,) + masked_cot.shape[1:])
    act_all = pieces[2].reshape((-1,) + activated.shape[1:])
    conv_shard, _ = lax.optimization_barrier((conv_weight, got))
    conv_kernel = lax.all_gather(conv_shard, "fsdp", axis=0, tiled=True).reshape(
        3, 3, channels, channels
    )

    conditioning = cond_table[bucket]
    conv_out = lax.conv_general_dilated(
        activated,
        conv_kernel,
        (1, 1),
        ((1, 1), (1, 1)),
        dimension_numbers=CONV_DIMS,
        preferred_element_type=jnp.float32,
    )
    conv_out = conv_out + conv_bias + conditioning[:, None, None, :]
    residual = (values + conv_out).astype(jnp.bfloat16)
    down_out = lax.conv_general_dilated(
        residual,
        down_kernel,
        (2, 2),
        ((1, 1), (1, 1)),
        dimension_numbers=CONV_DIMS,
        preferred_element_type=jnp.float32,
    )
    block_output = (down_out + down_bias).astype(jnp.bfloat16)
    block_output = jnp.where(live4, block_output, jnp.zeros_like(block_output))

    resid_all = lax.conv_general_dilated(
        cot_all,
        down_kernel[::-1, ::-1],
        (1, 1),
        ((1, 2), (1, 2)),
        lhs_dilation=(2, 2),
        dimension_numbers=BACK_DIMS,
        preferred_element_type=jnp.float32,
    )
    hid_all = resid_all.astype(jnp.bfloat16).reshape(-1, channels)
    grad_resid = lax.dynamic_slice_in_dim(
        resid_all, lax.axis_index("fsdp") * slot_total, slot_total, axis=0
    )
    grad_hidden = grad_resid.astype(jnp.bfloat16)
    grad_act = lax.conv_general_dilated(
        grad_hidden,
        conv_kernel[::-1, ::-1],
        (1, 1),
        ((1, 1), (1, 1)),
        dimension_numbers=BACK_DIMS,
        preferred_element_type=jnp.float32,
    )
    grad_pre = grad_act * sigmoid_v * (1.0 + pre_act * (1.0 - sigmoid_v))
    scaled = grad_pre * norm_gain
    mean_one = group_mean(jnp.sum(scaled, axis=(1, 2)), per_group)[:, None, None, :]
    mean_two = group_mean(jnp.sum(scaled * normed, axis=(1, 2)), per_group)[:, None, None, :]
    grad_input = (grad_resid + inv_std * (scaled - mean_one - normed * mean_two)).astype(
        jnp.bfloat16
    )
    affine = jnp.stack(
        [
            jnp.sum(grad_pre * normed, axis=(0, 1, 2)),
            jnp.sum(grad_pre, axis=(0, 1, 2)),
            jnp.sum(grad_resid, axis=(0, 1, 2)),
        ]
    )

    first_row = lax.axis_index("fsdp") * row_block
    first_tap = first_row // channels
    first_chan = first_row % channels
    span = (row_block + channels - 1) // channels + 1
    act_pad = jnp.pad(act_all, ((0, 0), (1, 1), (1, 1), (0, 0)))
    taps = [
        shifted(act_pad, jnp.minimum(first_tap + extra, 8), tile_side) for extra in range(span)
    ]
    tap_cols = jnp.concatenate(taps, axis=-1)
    own_cols = lax.dynamic_slice_in_dim(tap_cols, first_chan, row_block, axis=3)
    weight_term = lax.dot_general(
        own_cols.reshape(-1, row_block),
        hid_all,
        (((0,), (0,)), ((), ())),
        preferred_element_type=jnp.float32,
    )
    loss_scale = 4.0 / math.sqrt(
        tile_side * tile_side * slot_total * lax.axis_size("dp") * lax.axis_size("fsdp")
    )
    grad_conv = exchange_sum(weight_term * loss_scale, "dp")
    grad_affine = gathered_sum(gathered_sum(affine * loss_scale, "fsdp"), "dp")
    return (block_output, grad_input, grad_conv, grad_affine)


def solution(mesh):
    placed = (
        P(("dp", "fsdp"), None, None, None),
        P(("dp", "fsdp")),
        P(("dp", "fsdp"), None, None, None),
        P(("dp", "fsdp")),
        P(),
        P(),
        P(),
        P(),
        P(),
        P("fsdp", None),
        P("fsdp", None),
    )
    return jax.shard_map(
        body,
        mesh=mesh,
        in_specs=placed,
        out_specs=(
            P(("dp", "fsdp"), None, None, None),
            P(("dp", "fsdp"), None, None, None),
            P("fsdp", None),
            P(),
        ),
        check_vma=False,
    )
```

```python
import math

import jax
import jax.numpy as jnp
from jax import lax
from jax.sharding import PartitionSpec as P

GROUPS = 32
CONV_DIMS = ("NHWC", "HWIO", "NHWC")
BACK_DIMS = ("NHWC", "HWOI", "NHWC")


def group_mean(channel_sums, per_group):
    tiles, channels = channel_sums.shape
    width = channels // GROUPS
    grouped = channel_sums.reshape(tiles, GROUPS, width).sum(axis=-1) / per_group
    return jnp.repeat(grouped, width, axis=1)


def shifted(padded, tap, tile_side):
    row_off = tap // 3
    col_off = tap % 3
    return lax.dynamic_slice(
        padded,
        (0, row_off, col_off, 0),
        (padded.shape[0], tile_side, tile_side, padded.shape[3]),
    )


def halving_doubling_sum(block, axis):
    size = lax.axis_size(axis)
    levels = size.bit_length() - 1
    if size != 1 << levels or levels == 0:
        return lax.psum(block, axis)
    order = [0, levels - 1] + list(range(1, levels - 1)) if levels > 1 else [0]
    rows = block.shape[0]
    padded_rows = -(-rows // size) * size
    cur = jnp.pad(block, ((0, padded_rows - rows), (0, 0)))
    index = lax.axis_index(axis)
    for level in order:
        half = cur.shape[0] // 2
        low = ((index >> level) & 1) == 0
        send = jnp.where(low, cur[half:], cur[:half])
        keep = jnp.where(low, cur[:half], cur[half:])
        pairs = [(i, i ^ (1 << level)) for i in range(size)]
        cur = keep + lax.ppermute(send, axis, pairs)
    for level in reversed(order):
        low = ((index >> level) & 1) == 0
        pairs = [(i, i ^ (1 << level)) for i in range(size)]
        other = lax.ppermute(cur, axis, pairs)
        cur = jnp.where(low, jnp.concatenate([cur, other]), jnp.concatenate([other, cur]))
    return cur[:rows]


def doubling_sum(block, axis):
    size = lax.axis_size(axis)
    levels = size.bit_length() - 1
    if size != 1 << levels:
        return lax.psum(block, axis)
    for level in range(levels):
        pairs = [(i, i ^ (1 << level)) for i in range(size)]
        block = block + lax.ppermute(block, axis, pairs)
    return block


def exchange_sum(block, axis):
    size = lax.axis_size(axis)
    rows = block.shape[0]
    padded_rows = -(-rows // size) * size
    parts = jnp.pad(block, ((0, padded_rows - rows), (0, 0))).reshape(size, padded_rows // size, -1)
    mine = lax.all_to_all(parts, axis, 0, 0, tiled=False).sum(axis=0)
    spread = jnp.broadcast_to(mine[None], (size,) + mine.shape)
    full = lax.all_to_all(spread, axis, 0, 0, tiled=False)
    return full.reshape(padded_rows, -1)[:rows]


def gathered_sum(block, axis):
    size = lax.axis_size(axis)
    spread = jnp.broadcast_to(block[None], (size,) + block.shape)
    return lax.all_to_all(spread, axis, 0, 0, tiled=False).sum(axis=0)


def exchange_sum_with(block, extra, axis):
    size = lax.axis_size(axis)
    rows = block.shape[0]
    padded_rows = -(-rows // size) * size
    chunk = padded_rows // size
    parts = jnp.pad(block, ((0, padded_rows - rows), (0, 0))).reshape(size, chunk, -1)
    mine = lax.all_to_all(parts, axis, 0, 0, tiled=False).sum(axis=0)
    payload = jnp.concatenate([mine, extra], axis=0)
    spread = jnp.broadcast_to(payload[None], (size,) + payload.shape)
    full = lax.all_to_all(spread, axis, 0, 0, tiled=False)
    summed = full[:, :chunk].reshape(padded_rows, -1)[:rows]
    return summed, full[:, chunk:].sum(axis=0)


def body(
    latents,
    bucket,
    cotangent,
    tile_count,
    cond_table,
    norm_gain,
    norm_shift,
    conv_bias,
    down_bias,
    conv_weight,
    down_weight,
):
    slot_total, tile_side, _, channels = latents.shape
    row_block = conv_weight.shape[0]

    live = jnp.arange(slot_total, dtype=jnp.int32) < tile_count[0]
    live4 = live[:, None, None, None]
    masked_cot = jnp.where(live4, cotangent, jnp.zeros_like(cotangent))

    per_group = tile_side * tile_side * (channels // GROUPS)
    values = latents.astype(jnp.float32)
    center = group_mean(jnp.sum(values, axis=(1, 2)), per_group)
    deviation = values - center[:, None, None, :]
    spread = group_mean(jnp.sum(deviation * deviation, axis=(1, 2)), per_group)
    inv_std = lax.rsqrt(spread + 1e-05)[:, None, None, :]
    normed = deviation * inv_std
    pre_act = normed * norm_gain + norm_shift
    sigmoid_v = jax.nn.sigmoid(pre_act)
    activated = (pre_act * sigmoid_v).astype(jnp.bfloat16)
    cot_rows = masked_cot.reshape(-1, channels)
    act_rows = activated.reshape(-1, channels)
    first_parts = (down_weight, cot_rows, act_rows)
    got = lax.all_gather(jnp.concatenate(first_parts, axis=0), "fsdp", axis=0, tiled=False)
    edges = [0]
    for part in first_parts:
        edges.append(edges[-1] + part.shape[0])
    pieces = [got[:, edges[i] : edges[i + 1]] for i in range(len(first_parts))]
    down_kernel = pieces[0].reshape(3, 3, channels, channels)
    cot_all = pieces[1].reshape((-1,) + masked_cot.shape[1:])
    act_all = pieces[2].reshape((-1,) + activated.shape[1:])
    conv_shard, _ = lax.optimization_barrier((conv_weight, got))
    conv_kernel = lax.all_gather(conv_shard, "fsdp", axis=0, tiled=True).reshape(
        3, 3, channels, channels
    )

    conditioning = cond_table[bucket]
    conv_out = lax.conv_general_dilated(
        activated,
        conv_kernel,
        (1, 1),
        ((1, 1), (1, 1)),
        dimension_numbers=CONV_DIMS,
        preferred_element_type=jnp.float32,
    )
    conv_out = conv_out + conv_bias + conditioning[:, None, None, :]
    residual = (values + conv_out).astype(jnp.bfloat16)
    down_out = lax.conv_general_dilated(
        residual,
        down_kernel,
        (2, 2),
        ((1, 1), (1, 1)),
        dimension_numbers=CONV_DIMS,
        preferred_element_type=jnp.float32,
    )
    block_output = (down_out + down_bias).astype(jnp.bfloat16)
    block_output = jnp.where(live4, block_output, jnp.zeros_like(block_output))

    resid_all = lax.conv_general_dilated(
        cot_all,
        down_kernel[::-1, ::-1],
        (1, 1),
        ((1, 2), (1, 2)),
        lhs_dilation=(2, 2),
        dimension_numbers=BACK_DIMS,
        preferred_element_type=jnp.float32,
    )
    hid_all = resid_all.astype(jnp.bfloat16).reshape(-1, channels)
    grad_resid = lax.dynamic_slice_in_dim(
        resid_all, lax.axis_index("fsdp") * slot_total, slot_total, axis=0
    )
    grad_hidden = grad_resid.astype(jnp.bfloat16)
    grad_act = lax.conv_general_dilated(
        grad_hidden,
        conv_kernel[::-1, ::-1],
        (1, 1),
        ((1, 1), (1, 1)),
        dimension_numbers=BACK_DIMS,
        preferred_element_type=jnp.float32,
    )
    grad_pre = grad_act * sigmoid_v * (1.0 + pre_act * (1.0 - sigmoid_v))
    scaled = grad_pre * norm_gain
    mean_one = group_mean(jnp.sum(scaled, axis=(1, 2)), per_group)[:, None, None, :]
    mean_two = group_mean(jnp.sum(scaled * normed, axis=(1, 2)), per_group)[:, None, None, :]
    grad_input = (grad_resid + inv_std * (scaled - mean_one - normed * mean_two)).astype(
        jnp.bfloat16
    )
    affine = jnp.stack(
        [
            jnp.sum(grad_pre * normed, axis=(0, 1, 2)),
            jnp.sum(grad_pre, axis=(0, 1, 2)),
            jnp.sum(grad_resid, axis=(0, 1, 2)),
        ]
    )

    first_row = lax.axis_index("fsdp") * row_block
    first_tap = first_row // channels
    first_chan = first_row % channels
    span = (row_block + channels - 1) // channels + 1
    act_pad = jnp.pad(act_all, ((0, 0), (1, 1), (1, 1), (0, 0)))
    taps = [
        shifted(act_pad, jnp.minimum(first_tap + extra, 8), tile_side) for extra in range(span)
    ]
    tap_cols = jnp.concatenate(taps, axis=-1)
    own_cols = lax.dynamic_slice_in_dim(tap_cols, first_chan, row_block, axis=3)
    weight_term = lax.dot_general(
        own_cols.reshape(-1, row_block),
        hid_all,
        (((0,), (0,)), ((), ())),
        preferred_element_type=jnp.float32,
    )
    loss_scale = 4.0 / math.sqrt(
        tile_side * tile_side * slot_total * lax.axis_size("dp") * lax.axis_size("fsdp")
    )
    affine_fsdp = gathered_sum(affine * loss_scale, "fsdp")
    grad_conv, grad_affine = exchange_sum_with(weight_term * loss_scale, affine_fsdp, "dp")
    return (block_output, grad_input, grad_conv, grad_affine)


def solution(mesh):
    placed = (
        P(("dp", "fsdp"), None, None, None),
        P(("dp", "fsdp")),
        P(("dp", "fsdp"), None, None, None),
        P(("dp", "fsdp")),
        P(),
        P(),
        P(),
        P(),
        P(),
        P("fsdp", None),
        P("fsdp", None),
    )
    return jax.shard_map(
        body,
        mesh=mesh,
        in_specs=placed,
        out_specs=(
            P(("dp", "fsdp"), None, None, None),
            P(("dp", "fsdp"), None, None, None),
            P("fsdp", None),
            P(),
        ),
        check_vma=False,
    )
```
